32 devices in a mesh: rep: 2 (over y), ctx: 8 (over z, x), head: 2 (over core).
Axes of the slice: x: 2, y: 2, z: 4, core: 2. Of those that a mesh axis runs over, the one named last changes fastest.
Arguments:
- queries: bfloat16 [1024, 32, 128], P(('rep', 'ctx'), 'head'), parts along dimension 0, may hold values from -6 to 6
- keys: bfloat16 [1024, 4, 128], P(('rep', 'ctx'), 'head'), parts along dimension 0, may hold values from -6 to 6
- values: bfloat16 [1024, 4, 128], P(('rep', 'ctx'), 'head'), parts along dimension 0, may hold values from -6 to 6
Outputs:
- attended: bfloat16 [1024, 32, 128], P(('rep', 'ctx'), 'head'), parts along dimension 0
The draws below stay inside these ranges and needn't reach their ends.
There are 2 independent parts, one for each index of `rep`. The reference program is written for one: setup_inputs(seed, part) draws one part's arguments, and reference() takes and returns one part's arrays. A program takes and returns all parts, laid end to end along the dimension named above; each array names one. Nothing has to cross between parts.
All inputs are finite; a program needn't handle non-finite values.
Results may differ from the reference program's by a relative error of at most 0.0037.
Values may be sent and summed in bfloat16 or wider, within the bound.
No kernel may reach another device: no remote copies, remote signals or barrier semaphores. Data moves between devices by JAX's collectives and lax.ppermute only.
A program may use at most 128 MiB of HBM per device.

```python
import math
import jax
import jax.numpy as jnp
from jax import lax

HQ = 32
KEY_VALUE_HEADS = 4
HEAD_DIMENSION = 128
TOKEN_COUNT = 512


def draw_pair(key):
    query_key = jax.random.fold_in(key, 11)
    key_random_seed = jax.random.fold_in(key, 12)
    query_draw = jnp.clip(jax.random.normal(query_key, (TOKEN_COUNT, HQ, HEAD_DIMENSION), jnp.float32), -6.0, 6.0)
    key_sample = jnp.clip(jax.random.normal(key_random_seed, (TOKEN_COUNT, KEY_VALUE_HEADS, HEAD_DIMENSION), jnp.float32), -6.0, 6.0)
    return (query_draw, key_sample)


def draw_queries(key, part):
    return draw_pair(key)[0].astype(jnp.bfloat16)


def draw_keys(key, part):
    return draw_pair(key)[1].astype(jnp.bfloat16)


def shard_levels(own_key, extent, cuts, low, top_value):
    level = 1.0
    for axis_at, parts in cuts:
        steps = jax.random.uniform(jax.random.fold_in(jax.random.fold_in(own_key, 6), axis_at), (parts,), jnp.float32, low / len(cuts), top_value / len(cuts))
        level = level * jnp.repeat(jnp.exp(steps), extent[axis_at] // parts).reshape((-1,) + (1,) * (len(extent) - 1 - axis_at))
    return level


def noise(rng, extent, scale, limit, pieces=(), kind=jnp.bfloat16):
    drawn = scale * jax.random.normal(rng, extent, jnp.float32)
    if pieces:
        drawn = drawn * shard_levels(rng, extent, pieces, -0.22, 0.18)
    return jnp.clip(drawn, -limit, limit).astype(kind)


def setup_inputs(seed: int = 0, part: int = 0) -> dict:
    streams_of = jax.random.split(jax.random.key(seed), 4)
    part_keys = jax.random.split(jax.random.fold_in(streams_of[3], part), 4)
    return {
        "queries": draw_queries(jax.random.fold_in(jax.random.fold_in(streams_of[3], part), 71), part),
        "keys": draw_keys(jax.random.fold_in(jax.random.fold_in(streams_of[3], part), 71), part),
        "values": noise(part_keys[2], (TOKEN_COUNT, KEY_VALUE_HEADS, HEAD_DIMENSION), 1.0, 6.0, ((0, 8), (1, 2))),
    }


def reference(queries, keys, values):
    total_rows, query_heads, head_size = queries.shape
    key_heads = keys.shape[1]
    group_size = query_heads // key_heads
    key_float = keys.astype(jnp.float32)
    value_float = values.astype(jnp.float32)
    block_rows = math.gcd(total_rows, 256)
    scale = head_size ** -0.5
    key_position = jnp.arange(total_rows, dtype=jnp.int32)

    def one_block(which):
        start = (which * block_rows).astype(jnp.int32)
        rows = lax.dynamic_slice_in_dim(queries, start, block_rows, 0).astype(jnp.float32)
        rows = rows.reshape(block_rows, key_heads, group_size, head_size)
        scores = jnp.einsum('qhgd,khd->hgqk', rows, key_float) * scale
        query_position = start + jnp.arange(block_rows, dtype=jnp.int32)
        valid = key_position[None, :] <= query_position[:, None]
        scores = jnp.where(valid, scores, -1e30)
        row_max = jnp.max(scores, axis=-1, keepdims=True)
        raw = jnp.where(valid, jnp.exp(scores - row_max), 0.0)
        total = jnp.sum(raw, axis=-1)
        weights = lax.optimization_barrier(raw.astype(jnp.bfloat16)).astype(jnp.float32)
        summed = jnp.einsum('hgqk,khd->hgqd', weights, value_float)
        result = summed / total[..., None]
        result = jnp.transpose(result, (2, 0, 1, 3)).reshape(block_rows, query_heads, head_size)
        return result.astype(jnp.bfloat16)

    blocks = lax.map(one_block, jnp.arange(total_rows // block_rows, dtype=jnp.int32))
    return blocks.reshape(total_rows, query_heads, head_size)
```

```python
import jax
import jax.numpy as jnp
from jax import lax
from jax.sharding import PartitionSpec as P


def per_device(queries, keys, values):
    local_rows, query_heads, head_size = queries.shape
    key_heads = keys.shape[1]
    group_size = query_heads // key_heads
    scale = head_size ** (-0.5)
    context_size = lax.axis_size("ctx")
    me = lax.axis_index("ctx")
    offset = jnp.arange(local_rows, dtype=jnp.int32)
    position = me * local_rows + offset
    pair = jnp.concatenate([keys, values], axis=1)
    pieces = [pair]
    sources = [me * local_rows + offset]
    for shift in range(1, context_size):
        pieces.append(lax.ppermute(pair, "ctx", [(i, (i + shift) % context_size) for i in range(context_size)]))
        source = me - shift
        sources.append((source % context_size) * local_rows + offset)
    gathered = jnp.concatenate(pieces, axis=0)
    key_position = jnp.concatenate(sources, axis=0)
    key_all = gathered[:, :key_heads]
    value_all = gathered[:, key_heads:]
    rows = queries.reshape(local_rows, key_heads, group_size, head_size)
    scores = jnp.einsum("qhgd,khd->hgqk", rows, key_all, preferred_element_type=jnp.float32) * scale
    valid = key_position[None, :] <= position[:, None]
    scores = jnp.where(valid, scores, -1e30)
    row_max = jnp.max(scores, axis=-1)
    weights = jnp.where(valid, jnp.exp(scores - row_max[..., None]), 0.0)
    total = jnp.sum(weights, axis=-1)
    summed = jnp.einsum("hgqk,khd->hgqd", weights.astype(jnp.bfloat16), value_all,
                        preferred_element_type=jnp.float32)
    result = summed / total[..., None]
    result = jnp.transpose(result, (2, 0, 1, 3)).reshape(local_rows, query_heads, head_size)
    return result.astype(jnp.bfloat16)


def solution(mesh):
    placed = P(("rep", "ctx"), "head", None)
    return jax.shard_map(per_device, mesh=mesh, in_specs=(placed, placed, placed),
                         out_specs=placed, check_vma=False)
```

```python
import jax
import jax.numpy as jnp
from jax import lax
from jax.sharding import PartitionSpec as P


def per_device(queries, keys, values):
    local_rows, query_heads, head_size = queries.shape
    key_heads = keys.shape[1]
    group_size = query_heads // key_heads
    scale = head_size ** (-0.5)
    context_size = lax.axis_size("ctx")
    me = lax.axis_index("ctx")
    offset = jnp.arange(local_rows, dtype=jnp.int32)
    position = me * local_rows + offset
    pair = jnp.stack([keys, values], axis=0)
    pieces = [pair]
    sources = [me * local_rows + offset]
    for shift in range(1, context_size):
        pieces.append(lax.ppermute(pair, "ctx", [(i, (i + shift) % context_size) for i in range(context_size)]))
        source = me - shift
        sources.append((source % context_size) * local_rows + offset)
    gathered = jnp.concatenate(pieces, axis=1)
    key_position = jnp.concatenate(sources, axis=0)
    key_all = gathered[0]
    value_all = gathered[1]
    rows = queries.reshape(local_rows, key_heads, group_size, head_size)
    scores = jnp.einsum("qhgd,khd->hgqk", rows, key_all, preferred_element_type=jnp.float32) * scale
    valid = key_position[None, :] <= position[:, None]
    scores = jnp.where(valid, scores, -1e30)
    row_max = jnp.max(scores, axis=-1)
    weights = jnp.where(valid, jnp.exp(scores - row_max[..., None]), 0.0)
    total = jnp.sum(weights, axis=-1)
    summed = jnp.einsum("hgqk,khd->hgqd", weights.astype(jnp.bfloat16), value_all,
                        preferred_element_type=jnp.float32)
    result = summed / total[..., None]
    result = jnp.transpose(result, (2, 0, 1, 3)).reshape(local_rows, query_heads, head_size)
    return result.astype(jnp.bfloat16)


def solution(mesh):
    placed = P(("rep", "ctx"), "head", None)
    return jax.shard_map(per_device, mesh=mesh, in_specs=(placed, placed, placed),
                         out_specs=placed, check_vma=False)
```

```python
import jax
import jax.numpy as jnp
from jax import lax
from jax.sharding import PartitionSpec as P


def per_device(queries, keys, values):
    local_rows, query_heads, head_size = queries.shape
    key_heads = keys.shape[1]
    group_size = query_heads // key_heads
    scale = head_size ** (-0.5)
    context_size = lax.axis_size("ctx")
    me = lax.axis_index("ctx")
    offset = jnp.arange(local_rows, dtype=jnp.int32)
    position = me * local_rows + offset
    pair = jnp.stack([keys, values], axis=0)
    moved = {}
    after = {6: 1, 7: 2} if context_size == 8 else {}
    for shift in range(1, context_size):
        operand = pair
        if shift in after:
            operand = lax.optimization_barrier((pair, moved[after[shift]]))[0]
        moved[shift] = lax.ppermute(operand, "ctx", [(i, (i + shift) % context_size) for i in range(context_size)])
    order = [5, 4, 3, 2, 1, 6, 7] if context_size == 8 else list(range(1, context_size))
    pieces = [pair] + [moved[shift] for shift in order]
    sources = [me * local_rows + offset] + [((me - shift) % context_size) * local_rows + offset for shift in order]
    gathered = jnp.concatenate(pieces, axis=1)
    key_position = jnp.concatenate(sources, axis=0)
    key_all = gathered[0]
    value_all = gathered[1]
    rows = queries.reshape(local_rows, key_heads, group_size, head_size)
    scores = jnp.einsum("qhgd,khd->hgqk", rows, key_all, preferred_element_type=jnp.float32) * scale
    valid = key_position[None, :] <= position[:, None]
    scores = jnp.where(valid, scores, -1e30)
    row_max = jnp.max(scores, axis=-1)
    weights = jnp.exp(scores - row_max[..., None])
    total = jnp.sum(weights, axis=-1)
    summed = jnp.einsum("hgqk,khd->hgqd", weights.astype(jnp.bfloat16), value_all,
                        preferred_element_type=jnp.float32)
    result = summed / total[..., None]
    result = jnp.transpose(result, (2, 0, 1, 3)).reshape(local_rows, query_heads, head_size)
    return result.astype(jnp.bfloat16)


def solution(mesh):
    placed = P(("rep", "ctx"), "head", None)
    return jax.shard_map(per_device, mesh=mesh, in_specs=(placed, placed, placed),
                         out_specs=placed, check_vma=False)
```

```python
import jax
import jax.numpy as jnp
from jax import lax
from jax.experimental.layout import Layout, with_layout_constraint
from jax.sharding import PartitionSpec as P


def per_device(queries, keys, values):
    local_rows, query_heads, head_size = queries.shape
    key_heads = keys.shape[1]
    group_size = query_heads // key_heads
    scale = head_size ** (-0.5)
    context_size = lax.axis_size("ctx")
    me = lax.axis_index("ctx")
    offset = jnp.arange(local_rows, dtype=jnp.int32)
    position = me * local_rows + offset
    pair = jnp.stack([keys, values], axis=0)
    moved = {}
    after = {6: 1, 7: 2} if context_size == 8 else {}
    for shift in range(1, context_size):
        operand = pair
        if shift in after:
            operand = lax.optimization_barrier((pair, moved[after[shift]]))[0]
        moved[shift] = lax.ppermute(operand, "ctx", [(i, (i + shift) % context_size) for i in range(context_size)])
    order = [5, 4, 3, 2, 1, 6, 7] if context_size == 8 else list(range(1, context_size))
    pieces = [pair] + [moved[shift] for shift in order]
    sources = [me * local_rows + offset] + [((me - shift) % context_size) * local_rows + offset for shift in order]
    gathered = jnp.concatenate(pieces, axis=1)
    key_position = jnp.concatenate(sources, axis=0)
    key_all = gathered[0]
    value_all = gathered[1]
    rows = queries.reshape(local_rows, key_heads, group_size, head_size)
    scores = jnp.einsum("qhgd,khd->hgqk", rows, key_all, preferred_element_type=jnp.float32) * scale
    valid = key_position[None, :] <= position[:, None]
    scores = jnp.where(valid, scores, -1e30)
    row_max = jnp.max(scores, axis=-1)
    weights = jnp.exp(scores - row_max[..., None])
    total = jnp.sum(weights, axis=-1)
    summed = jnp.einsum("hgqk,khd->hgqd", weights.astype(jnp.bfloat16), value_all,
                        preferred_element_type=jnp.float32)
    summed = with_layout_constraint(summed, Layout((2, 0, 1, 3)))
    result = summed / total[..., None]
    result = jnp.transpose(result, (2, 0, 1, 3)).reshape(local_rows, query_heads, head_size)
    return result.astype(jnp.bfloat16)


def solution(mesh):
    placed = P(("rep", "ctx"), "head", None)
    return jax.shard_map(per_device, mesh=mesh, in_specs=(placed, placed, placed),
                         out_specs=placed, check_vma=False)
```

```python
import jax
import jax.numpy as jnp
from jax import lax
from jax.experimental.layout import Layout, with_layout_constraint
from jax.sharding import PartitionSpec as P


def per_device(queries, keys, values):
    local_rows, query_heads, head_size = queries.shape
    key_heads = keys.shape[1]
    group_size = query_heads // key_heads
    scale = head_size ** (-0.5)
    context_size = lax.axis_size("ctx")
    me = lax.axis_index("ctx")
    offset = jnp.arange(local_rows, dtype=jnp.int32)
    position = me * local_rows + offset
    pair = jnp.stack([keys, values], axis=0)
    moved = {}
    after = {6: 1, 7: 2} if context_size == 8 else {}
    for shift in range(1, context_size):
        operand = pair
        if shift in after:
            operand = lax.optimization_barrier((pair, moved[after[shift]]))[0]
        moved[shift] = lax.ppermute(operand, "ctx", [(i, (i + shift) % context_size) for i in range(context_size)])
    order = [5, 4, 3, 2, 1, 6, 7] if context_size == 8 else list(range(1, context_size))
    pieces = [pair] + [moved[shift] for shift in order]
    sources = [me * local_rows + offset] + [((me - shift) % context_size) * local_rows + offset for shift in order]
    gathered = jnp.concatenate(pieces, axis=1)
    key_position = jnp.concatenate(sources, axis=0)
    key_all = gathered[0]
    value_all = gathered[1]
    rows = queries.reshape(local_rows, key_heads, group_size, head_size)
    scores = jnp.einsum("qhgd,khd->hgqk", rows, key_all, preferred_element_type=jnp.float32) * scale
    valid = key_position[None, :] <= position[:, None]
    scores = jnp.where(valid, scores, -1e30)
    early = [1, 2] if context_size == 8 else []
    late = [3, 4, 5, 6, 7] if context_size == 8 else [shift for shift in order if shift not in early]
    part_max = []
    for part in ([0] + early, late):
        part_keys = jnp.concatenate([pieces[0] if shift == 0 else moved[shift] for shift in part], axis=1)[0]
        part_position = jnp.concatenate(
            [((me - shift) % context_size) * local_rows + offset for shift in part], axis=0)
        part_scores = jnp.einsum("qhgd,khd->hgqk", rows, part_keys, preferred_element_type=jnp.float32) * scale
        part_valid = part_position[None, :] <= position[:, None]
        part_max.append(jnp.max(jnp.where(part_valid, part_scores, -1e30), axis=-1))
    row_max = jnp.maximum(part_max[0], part_max[1])
    weights = jnp.exp(scores - row_max[..., None])
    total = jnp.sum(weights, axis=-1)
    summed = jnp.einsum("hgqk,khd->hgqd", weights.astype(jnp.bfloat16), value_all,
                        preferred_element_type=jnp.float32)
    summed = with_layout_constraint(summed, Layout((2, 0, 1, 3)))
    result = summed / total[..., None]
    result = jnp.transpose(result, (2, 0, 1, 3)).reshape(local_rows, query_heads, head_size)
    return result.astype(jnp.bfloat16)


def solution(mesh):
    placed = P(("rep", "ctx"), "head", None)
    return jax.shard_map(per_device, mesh=mesh, in_specs=(placed, placed, placed),
                         out_specs=placed, check_vma=False)
```

```python
import jax
import jax.numpy as jnp
from jax import lax
from jax.experimental.layout import Layout, with_layout_constraint
from jax.sharding import PartitionSpec as P


def per_device(queries, keys, values):
    local_rows, query_heads, head_size = queries.shape
    key_heads = keys.shape[1]
    group_size = query_heads // key_heads
    scale = head_size ** (-0.5)
    context_size = lax.axis_size("ctx")
    me = lax.axis_index("ctx")
    offset = jnp.arange(local_rows, dtype=jnp.int32)
    position = me * local_rows + offset
    pair = jnp.stack([keys, values], axis=0)
    moved = {}
    after = {6: 1, 7: 2} if context_size == 8 else {}
    for shift in range(1, context_size):
        operand = pair
        if shift in after:
            operand = lax.optimization_barrier((pair, moved[after[shift]]))[0]
        moved[shift] = lax.ppermute(operand, "ctx", [(i, (i + shift) % context_size) for i in range(context_size)])
    order = [5, 4, 3, 2, 1, 6, 7] if context_size == 8 else list(range(1, context_size))
    pieces = [pair] + [moved[shift] for shift in order]
    sources = [me * local_rows + offset] + [((me - shift) % context_size) * local_rows + offset for shift in order]
    gathered = jnp.concatenate(pieces, axis=1)
    key_position = jnp.concatenate(sources, axis=0)
    key_all = gathered[0]
    value_all = gathered[1]
    rows = queries.reshape(local_rows, key_heads, group_size, head_size)
    scores = jnp.einsum("qhgd,khd->hgqk", rows, key_all, preferred_element_type=jnp.float32)
    valid = key_position[None, :] <= position[:, None]
    scores = jnp.where(valid, scores, -1e30)
    row_max = jnp.max(scores, axis=-1)
    weights = jnp.exp((scores - row_max[..., None]) * scale)
    total = jnp.sum(weights, axis=-1)
    summed = jnp.einsum("hgqk,khd->hgqd", weights.astype(jnp.bfloat16), value_all,
                        preferred_element_type=jnp.float32)
    summed = with_layout_constraint(summed, Layout((2, 0, 1, 3)))
    result = summed / total[..., None]
    result = jnp.transpose(result, (2, 0, 1, 3)).reshape(local_rows, query_heads, head_size)
    return result.astype(jnp.bfloat16)


def solution(mesh):
    placed = P(("rep", "ctx"), "head", None)
    return jax.shard_map(per_device, mesh=mesh, in_specs=(placed, placed, placed),
                         out_specs=placed, check_vma=False)
```

```python
import jax
import jax.numpy as jnp
from jax import lax
from jax.experimental.layout import Layout, with_layout_constraint
from jax.sharding import PartitionSpec as P


def per_device(queries, keys, values):
    local_rows, query_heads, head_size = queries.shape
    key_heads = keys.shape[1]
    group_size = query_heads // key_heads
    scale = head_size ** (-0.5)
    context_size = lax.axis_size("ctx")
    me = lax.axis_index("ctx")
    offset = jnp.arange(local_rows, dtype=jnp.int32)
    position = me * local_rows + offset
    pair = jnp.stack([keys, values], axis=0)
    moved = {}
    after = {6: 1, 7: 2} if context_size == 8 else {}
    for shift in range(1, context_size):
        operand = pair
        if shift in after:
            operand = lax.optimization_barrier((pair, moved[after[shift]]))[0]
        moved[shift] = lax.ppermute(operand, "ctx", [(i, (i + shift) % context_size) for i in range(context_size)])
    order = [5, 4, 3, 2, 1, 6, 7] if context_size == 8 else list(range(1, context_size))
    pieces = [pair] + [moved[shift] for shift in order]
    sources = [me * local_rows + offset] + [((me - shift) % context_size) * local_rows + offset for shift in order]
    gathered = jnp.concatenate(pieces, axis=1)
    key_position = jnp.concatenate(sources, axis=0)
    key_all = gathered[0]
    value_all = gathered[1]
    rows = queries.reshape(local_rows, key_heads, group_size, head_size)
    scores = jnp.einsum("qhgd,khd->hgqk", rows, key_all, preferred_element_type=jnp.float32) * scale
    valid = key_position[None, :] <= position[:, None]
    scores = lax.optimization_barrier(jnp.where(valid, scores, -1e30))
    row_max = jnp.max(scores, axis=-1)
    weights = jnp.exp(scores - row_max[..., None])
    total = jnp.sum(weights, axis=-1)
    summed = jnp.einsum("hgqk,khd->hgqd", weights.astype(jnp.bfloat16), value_all,
                        preferred_element_type=jnp.float32)
    summed = with_layout_constraint(summed, Layout((2, 0, 1, 3)))
    result = summed / total[..., None]
    result = jnp.transpose(result, (2, 0, 1, 3)).reshape(local_rows, query_heads, head_size)
    return result.astype(jnp.bfloat16)


def solution(mesh):
    placed = P(("rep", "ctx"), "head", None)
    return jax.shard_map(per_device, mesh=mesh, in_specs=(placed, placed, placed),
                         out_specs=placed, check_vma=False)
```

```python
import jax
import jax.numpy as jnp
from jax import lax
from jax.experimental.layout import Layout, with_layout_constraint
from jax.sharding import PartitionSpec as P


def per_device(queries, keys, values):
    local_rows, query_heads, head_size = queries.shape
    key_heads = keys.shape[1]
    group_size = query_heads // key_heads
    scale = head_size ** (-0.5)
    context_size = lax.axis_size("ctx")
    me = lax.axis_index("ctx")
    offset = jnp.arange(local_rows, dtype=jnp.int32)
    position = me * local_rows + offset
    pair = jnp.stack([keys, values], axis=0)
    moved = {}
    after = {7: 1, 6: 2} if context_size == 8 else {}
    for shift in range(1, context_size):
        operand = pair
        if shift in after:
            operand = lax.optimization_barrier((pair, moved[after[shift]]))[0]
        moved[shift] = lax.ppermute(operand, "ctx", [(i, (i + shift) % context_size) for i in range(context_size)])
    order = [5, 4, 3, 2, 1, 7, 6] if context_size == 8 else list(range(1, context_size))
    pieces = [pair] + [moved[shift] for shift in order]
    sources = [me * local_rows + offset] + [((me - shift) % context_size) * local_rows + offset for shift in order]
    gathered = jnp.concatenate(pieces, axis=1)
    key_position = jnp.concatenate(sources, axis=0)
    key_all = gathered[0]
    value_all = gathered[1]
    rows = queries.reshape(local_rows, key_heads, group_size, head_size)
    scores = jnp.einsum("qhgd,khd->hgqk", rows, key_all, preferred_element_type=jnp.float32) * scale
    valid = key_position[None, :] <= position[:, None]
    scores = jnp.where(valid, scores, -1e30)
    row_max = jnp.max(scores, axis=-1)
    weights = jnp.exp(scores - row_max[..., None])
    total = jnp.sum(weights, axis=-1)
    summed = jnp.einsum("hgqk,khd->hgqd", weights.astype(jnp.bfloat16), value_all,
                        preferred_element_type=jnp.float32)
    summed = with_layout_constraint(summed, Layout((2, 0, 1, 3)))
    result = summed / total[..., None]
    result = jnp.transpose(result, (2, 0, 1, 3)).reshape(local_rows, query_heads, head_size)
    return result.astype(jnp.bfloat16)


def solution(mesh):
    placed = P(("rep", "ctx"), "head", None)
    return jax.shard_map(per_device, mesh=mesh, in_specs=(placed, placed, placed),
                         out_specs=placed, check_vma=False)
```

```python
import jax
import jax.numpy as jnp
from jax import lax
from jax.experimental.layout import Layout, with_layout_constraint
from jax.sharding import PartitionSpec as P


def per_device(queries, keys, values):
    local_rows, query_heads, head_size = queries.shape
    key_heads = keys.shape[1]
    group_size = query_heads // key_heads
    scale = head_size ** (-0.5)
    context_size = lax.axis_size("ctx")
    me = lax.axis_index("ctx")
    offset = jnp.arange(local_rows, dtype=jnp.int32)
    position = me * local_rows + offset
    pair = jnp.stack([keys, values], axis=0)
    moved = {}
    steps = {1: (0, 1), 2: (1, 0), 3: (1, 1), 4: (2, 0), 5: (2, 1), 6: (3, 0), 7: (3, 1)}
    after = {6: 1, 7: 2} if context_size == 8 else {}
    for shift in range(1, context_size):
        operand = pair
        if shift in after:
            operand = lax.optimization_barrier((pair, moved[after[shift]]))[0]
        pairs = [(i, (i + shift) % context_size) for i in range(context_size)]
        if context_size == 8:
            move, flip = steps[shift]
            pairs = [(i, 2 * ((i // 2 + move) % 4) + (i % 2 ^ flip)) for i in range(context_size)]
        moved[shift] = lax.ppermute(operand, "ctx", pairs)
    order = [5, 4, 3, 2, 1, 6, 7] if context_size == 8 else list(range(1, context_size))
    pieces = [pair] + [moved[shift] for shift in order]
    def source(shift):
        if context_size == 8:
            move, flip = steps[shift]
            return 2 * ((me // 2 - move) % 4) + (me % 2 ^ flip)
        return (me - shift) % context_size
    sources = [me * local_rows + offset] + [source(shift) * local_rows + offset for shift in order]
    gathered = jnp.concatenate(pieces, axis=1)
    key_position = jnp.concatenate(sources, axis=0)
    key_all = gathered[0]
    value_all = gathered[1]
    rows = queries.reshape(local_rows, key_heads, group_size, head_size)
    scores = jnp.einsum("qhgd,khd->hgqk", rows, key_all, preferred_element_type=jnp.float32) * scale
    valid = key_position[None, :] <= position[:, None]
    scores = jnp.where(valid, scores, -1e30)
    row_max = jnp.max(scores, axis=-1)
    weights = jnp.exp(scores - row_max[..., None])
    total = jnp.sum(weights, axis=-1)
    summed = jnp.einsum("hgqk,khd->hgqd", weights.astype(jnp.bfloat16), value_all,
                        preferred_element_type=jnp.float32)
    summed = with_layout_constraint(summed, Layout((2, 0, 1, 3)))
    result = summed / total[..., None]
    result = jnp.transpose(result, (2, 0, 1, 3)).reshape(local_rows, query_heads, head_size)
    return result.astype(jnp.bfloat16)


def solution(mesh):
    placed = P(("rep", "ctx"), "head", None)
    return jax.shard_map(per_device, mesh=mesh, in_specs=(placed, placed, placed),
                         out_specs=placed, check_vma=False)
```
